256 devices in a mesh: dp: 16 (over z_lo, y, core), tensor: 16 (over z_hi, x).
Axes of the slice: x: 4, y: 4, z: 8 (z_hi: 4, z_lo: 2; z = z_hi * 2 + z_lo), core: 2. Of those that a mesh axis runs over, the one named last changes fastest.
Arguments:
- attn_in: bfloat16 [4096, 4096], P('dp', 'tensor'), parts along dimension 0, may hold values from -127 to 127
- wo_int: bfloat16 [4096, 8192], P('tensor'), may hold values from -127 to 127
- wo_exponent: int32 [8192], replicated, may hold values from -15 to -12
- token_scale: float32 [4096], P(('dp', 'tensor')), parts along dimension 0, may hold values from 0.3 to 3
- residual: bfloat16 [4096, 8192], P(('dp', 'tensor')), parts along dimension 0, may hold values from -6 to 6
- norm_gain: float32 [8192], replicated, may hold values from 0.5 to 1.5
- gate_int: bfloat16 [8192, 4096], P(None, 'tensor'), may hold values from -127 to 127, as said below
- up_int: bfloat16 [8192, 4096], P(None, 'tensor'), may hold values from -127 to 127, as said below
- gate_exponent: int32 [4096], P('tensor'), may hold values from -14 to -12
- up_exponent: int32 [4096], P('tensor'), may hold values from -14 to -12
Outputs:
- hidden: bfloat16 [4096, 4096], P('dp', 'tensor'), parts along dimension 0
- checksum: float32 [256, 8192], P(('dp', 'tensor')), parts along dimension 0
The draws below stay inside these ranges and needn't reach their ends.
There are 16 independent parts, one for each index of `dp`. The reference program is written for one: setup_inputs(seed, part) draws one part's arguments, and reference() takes and returns one part's arrays. A program takes and returns all parts, laid end to end along the dimension named above; an argument that names none is the same for every part. Nothing has to cross between parts.
Inputs may be any that keep to these rules, and one draw needn't show every extreme that they name: `gate_int`: integer values. `up_int`: integer values.
All inputs are finite; a program needn't handle non-finite values.
Results may differ from the reference program's by a relative error of at most 0.035.
Values may be sent and summed in bfloat16 or wider, within the bound.
No kernel may reach another device: no remote copies, remote signals or barrier semaphores. Data moves between devices by JAX's collectives and lax.ppermute only.
A program may use at most 64 MiB of HBM per device.

```python
import math
import jax
import jax.numpy as jnp
from jax import lax

D = 8192
D_LOG = 13
TOK_DEV = 16
TOKENS = 256
HW = 4096
FF_WIN = 4096
N_TENSOR = 16


def int_table(key, shape):
    return jax.random.randint(key, shape, -127, 128).astype(jnp.float32).astype(jnp.bfloat16)


def draw_attn_in(key, part):
    first, second, third, fourth = jax.random.split(jax.random.fold_in(key, 3), 4)
    half_width = HW // 2
    amplitude = jax.random.randint(first, (TOKENS, 1), 32, 128)
    nudges = jax.random.randint(third, (TOKENS, half_width), -2, 3)
    raw_bits = jax.random.randint(second, (TOKENS, half_width), 0, 65536)
    values = raw_bits * (2 * amplitude + 1) // 65536 - amplitude
    partner = jnp.clip(values + nudges, -127, 127)
    joined = jnp.concatenate([values, partner], axis=1).astype(jnp.float32)
    jitter = jax.random.uniform(fourth, (TOKENS, HW), jnp.float32, -1.0, 1.0)
    return jnp.clip(joined + jitter, -127.0, 127.0).astype(jnp.bfloat16)


def draw_wo_int(key, part):
    first, second, third = jax.random.split(jax.random.fold_in(key, 5), 3)
    half_width = HW // 2
    base_rows = jax.random.randint(first, (half_width, D), -120, 121)
    errors = jax.random.randint(second, (half_width, D), -6, 7)
    joined = jnp.concatenate([base_rows, errors - base_rows], axis=0).astype(jnp.float32)
    jitter = jax.random.uniform(third, (HW, D), jnp.float32, -1.0, 1.0)
    return jnp.clip(joined + jitter, -127.0, 127.0).astype(jnp.bfloat16)


def draw_gate_int(key, part):
    return int_table(jax.random.fold_in(key, 7), (D, FF_WIN))


def draw_up_int(key, part):
    return int_table(jax.random.fold_in(key, 11), (D, FF_WIN))


def touch_ends(result, stream_key, smallest, high):
    longest = result.shape.index(max(result.shape))
    spots = []
    for shift in (0, 1):
        where = [jax.random.randint(jax.random.fold_in(stream_key, axis), (), 0, length) for axis, length in enumerate(result.shape)]
        where[longest] = (where[longest] + shift) % result.shape[longest]
        spots.append(tuple(where))
    return result.at[spots[0]].set(smallest).at[spots[1]].set(high)


def steps_of(stream_key, extent, cuts, low, high):
    def one(axis_at, blocks):
        steps = jax.random.uniform(jax.random.fold_in(jax.random.fold_in(stream_key, 6), axis_at), (blocks,), jnp.float32, low / len(cuts), high / len(cuts))
        return jnp.repeat(jnp.exp(steps), extent[axis_at] // blocks).reshape((-1,) + (1,) * (len(extent) - axis_at - 1))

    factor_of = one(*cuts[0])
    for cut in cuts[1:]:
        factor_of = factor_of * one(*cut)
    return factor_of


def bell_draw(own_key, dims, spread, reach, cuts=(), held_as=jnp.bfloat16):
    drawn = spread * jax.random.normal(own_key, dims, jnp.float32)
    if cuts:
        drawn = drawn * steps_of(own_key, dims, cuts, -0.22, 0.18)
    return jnp.clip(drawn, -reach, reach).astype(held_as)


def setup_inputs(seed: int = 0, part: int = 0) -> dict:
    key_list = jax.random.split(jax.random.key(seed), 11)
    part_keys = jax.random.split(jax.random.fold_in(key_list[10], part), 11)
    attn_in = draw_attn_in(jax.random.fold_in(jax.random.fold_in(key_list[10], part), 71), part)
    wo_int = draw_wo_int(jax.random.fold_in(key_list[10], 71), part)
    wo_exponent = touch_ends(jax.random.randint(key_list[2], (D,), D_LOG // 3 - 19, D_LOG // 3 - 15), jax.random.fold_in(key_list[2], 1), D_LOG // 3 - 19, (D_LOG // 3 - 15) - 1).astype(jnp.int32)
    token_scale = jnp.clip(jnp.exp(math.log(3.0) - 2.3025851 * jax.random.uniform(part_keys[3], (TOKENS,), jnp.float32) ** steps_of(part_keys[3], (TOKENS,), ((0, 16),), -0.2, 0.2)), 0.3, 3.0)
    residual = bell_draw(part_keys[4], (TOKENS, D), 1.0, 6.0, ((0, 16),))
    norm_gain = jnp.clip(1.0 + 0.1 * jax.random.normal(key_list[5], (D,), jnp.float32), 0.5, 1.5)
    gate_int = draw_gate_int(jax.random.fold_in(key_list[10], 71), part)
    up_int = draw_up_int(jax.random.fold_in(key_list[10], 71), part)
    gate_exponent = touch_ends(jax.random.randint(key_list[8], (FF_WIN,), -8 - D_LOG // 2, -5 - D_LOG // 2), jax.random.fold_in(key_list[8], 1), -8 - D_LOG // 2, (-5 - D_LOG // 2) - 1).astype(jnp.int32)
    up_exponent = touch_ends(jax.random.randint(key_list[9], (FF_WIN,), -8 - D_LOG // 2, -5 - D_LOG // 2), jax.random.fold_in(key_list[9], 1), -8 - D_LOG // 2, (-5 - D_LOG // 2) - 1).astype(jnp.int32)
    return {"attn_in": attn_in, "wo_int": wo_int, "wo_exponent": wo_exponent, "token_scale": token_scale, "residual": residual, "norm_gain": norm_gain, "gate_int": gate_int, "up_int": up_int, "gate_exponent": gate_exponent, "up_exponent": up_exponent}


def normalize(stream, norm_gain):
    widened = stream.astype(jnp.float32)
    inverse = lax.rsqrt(lax.optimization_barrier(jnp.mean(widened * widened, axis=1, keepdims=True)) + 1e-05)
    return (widened * inverse * norm_gain[None, :]).astype(jnp.bfloat16)

def quantize(normed_low):
    widened = lax.optimization_barrier(normed_low).astype(jnp.float32)
    largest = lax.optimization_barrier(jnp.max(jnp.abs(widened), axis=1, keepdims=True))
    xscale = ((largest + 1e-06) / 127.0).astype(jnp.bfloat16)
    levels = jnp.floor(widened / xscale.astype(jnp.float32) + 0.5).astype(jnp.bfloat16)
    return (levels, xscale)

def reference(attn_in, wo_int, wo_exponent, token_scale, residual, norm_gain, gate_int, up_int, gate_exponent, up_exponent):
    proj_int = jnp.dot(attn_in, wo_int, preferred_element_type=jnp.float32)
    col_scale = jnp.exp2(wo_exponent.astype(jnp.float32))
    blocks = proj_int.reshape(N_TENSOR, TOK_DEV, D)
    checksum = lax.optimization_barrier(jnp.sum(blocks, axis=1)) * col_scale[None, :] / TOK_DEV
    attn_out = proj_int * token_scale[:, None] * col_scale[None, :]
    stream = (residual.astype(jnp.float32) + attn_out).astype(jnp.bfloat16)
    levels, xscale = quantize(normalize(stream, norm_gain))
    row_scale = xscale.astype(jnp.float32)
    gate_scale = jnp.exp2(gate_exponent.astype(jnp.float32))[None, :]
    up_scale = jnp.exp2(up_exponent.astype(jnp.float32))[None, :]
    gate_sum = jnp.dot(levels, gate_int, preferred_element_type=jnp.float32) * row_scale * gate_scale
    up_sum = jnp.dot(levels, up_int, preferred_element_type=jnp.float32) * row_scale * up_scale
    hidden = (jax.nn.silu(gate_sum) * up_sum).astype(jnp.bfloat16)
    return (hidden, checksum)
```

```python
import jax
import jax.numpy as jnp
from jax import lax
from jax.sharding import PartitionSpec as P


def normalize(stream, norm_gain):
    widened = stream.astype(jnp.float32)
    inverse = lax.rsqrt(jnp.mean(widened * widened, axis=1, keepdims=True) + 1e-05)
    return (widened * inverse * norm_gain[None, :]).astype(jnp.bfloat16)


def quantize(normed_low):
    widened = lax.optimization_barrier(normed_low).astype(jnp.float32)
    largest = jnp.max(jnp.abs(widened), axis=1, keepdims=True)
    xscale = ((largest + 1e-06) / 127.0).astype(jnp.bfloat16)
    levels = jnp.floor(widened / xscale.astype(jnp.float32) + 0.5).astype(jnp.bfloat16)
    return (levels, xscale)


def local(
    attn_in,
    wo_int,
    wo_exponent,
    token_scale,
    residual,
    norm_gain,
    gate_int,
    up_int,
    gate_exponent,
    up_exponent,
):
    own_rows = residual.shape[0]
    col_scale = jnp.exp2(wo_exponent.astype(jnp.float32))
    gate_scale = jnp.exp2(gate_exponent.astype(jnp.float32))[None, :]
    up_scale = jnp.exp2(up_exponent.astype(jnp.float32))[None, :]
    partial_value = jnp.dot(attn_in, wo_int, preferred_element_type=jnp.float32)
    owned_rows = lax.psum_scatter(partial_value, "tensor", scatter_dimension=0, tiled=True)
    col_total = jnp.sum(owned_rows, axis=0, keepdims=True)
    checksum = col_total * col_scale[None, :] / own_rows
    attn_out = owned_rows * token_scale[:, None] * col_scale[None, :]
    stream = (residual.astype(jnp.float32) + attn_out).astype(jnp.bfloat16)
    normed_low = normalize(stream, norm_gain)
    all_normed = lax.all_gather(normed_low, "tensor", axis=0, tiled=True)
    levels, xscale = quantize(all_normed)
    row_scale = xscale.astype(jnp.float32)
    gate_sum = (
        jnp.dot(levels, gate_int, preferred_element_type=jnp.float32) * row_scale * gate_scale
    )
    up_sum = jnp.dot(levels, up_int, preferred_element_type=jnp.float32) * row_scale * up_scale
    hidden = (jax.nn.silu(gate_sum) * up_sum).astype(jnp.bfloat16)
    return (hidden, checksum)


def solution(mesh):
    placed = (
        P("dp", "tensor"),
        P("tensor", None),
        P(),
        P(("dp", "tensor")),
        P(("dp", "tensor"), None),
        P(),
        P(None, "tensor"),
        P(None, "tensor"),
        P("tensor"),
        P("tensor"),
    )
    return jax.shard_map(
        local,
        mesh=mesh,
        in_specs=placed,
        out_specs=(P("dp", "tensor"), P(("dp", "tensor"), None)),
        check_vma=False,
    )
```

```python
import jax
import jax.numpy as jnp
from jax import lax
from jax.sharding import PartitionSpec as P

X_RING = 4
SCALE_COLS = 128


def ring_perm(groups, axis, shift):
    pairs = []
    for t in range(groups):
        z, x = divmod(t, X_RING)
        if axis == "x":
            dst = z * X_RING + (x + shift) % X_RING
        else:
            dst = ((z + shift) % (groups // X_RING)) * X_RING + x
        pairs.append((t, dst))
    return pairs


def ring_reduce_scatter(parts, groups, axis, chunk_axis):
    n = parts.shape[chunk_axis]
    half = parts.shape[-1] // 2
    left = parts[..., :half]
    right = parts[..., half:]
    take = lambda arr, j: lax.index_in_dim(arr, j % n, axis=chunk_axis, keepdims=False)
    fwd = ring_perm(groups, axis, 1)
    bwd = ring_perm(groups, axis, -1)
    acc_f = take(left, n - 1)
    acc_b = take(right, 1)
    for s in range(n - 1):
        got_f = lax.ppermute(acc_f, "tensor", fwd)
        got_b = lax.ppermute(acc_b, "tensor", bwd)
        acc_f = got_f + take(left, n - 2 - s)
        acc_b = got_b + take(right, s + 2)
    return jnp.concatenate([acc_f, acc_b], axis=-1)


def ring_all_gather(block, groups, axis, split):
    n = X_RING if axis == "x" else groups // X_RING
    fwd = ring_perm(groups, axis, 1)
    bwd = ring_perm(groups, axis, -1)
    left = [None] * n
    right = [None] * n
    left[0] = block[..., :split]
    right[0] = block[..., split:]
    cur_f = left[0]
    cur_b = right[0]
    for s in range(n - 1):
        cur_f = lax.ppermute(cur_f, "tensor", fwd)
        cur_b = lax.ppermute(cur_b, "tensor", bwd)
        left[n - 1 - s] = cur_f
        right[s + 1] = cur_b
    return jnp.stack([jnp.concatenate([a, b], axis=-1) for a, b in zip(left, right)])


def normalize(stream, norm_gain):
    widened = stream.astype(jnp.float32)
    inverse = lax.rsqrt(jnp.mean(widened * widened, axis=1, keepdims=True) + 1e-05)
    return (widened * inverse * norm_gain[None, :]).astype(jnp.bfloat16)


def quantize(normed_low):
    widened = lax.optimization_barrier(normed_low).astype(jnp.float32)
    largest = jnp.max(jnp.abs(widened), axis=1, keepdims=True)
    xscale = ((largest + 1e-06) / 127.0).astype(jnp.bfloat16)
    levels = jnp.floor(widened / xscale.astype(jnp.float32) + 0.5).astype(jnp.bfloat16)
    return (levels, xscale)


def local(
    attn_in,
    wo_int,
    wo_exponent,
    token_scale,
    residual,
    norm_gain,
    gate_int,
    up_int,
    gate_exponent,
    up_exponent,
):
    groups = lax.axis_size("tensor")
    nz = groups // X_RING
    own_rows = residual.shape[0]
    width = wo_int.shape[1]
    me = lax.axis_index("tensor")
    my_z = me // X_RING
    my_x = me % X_RING
    col_scale = jnp.exp2(wo_exponent.astype(jnp.float32))
    gate_scale = jnp.exp2(gate_exponent.astype(jnp.float32))[None, :]
    up_scale = jnp.exp2(up_exponent.astype(jnp.float32))[None, :]

    rows = attn_in.reshape(nz, X_RING, own_rows, attn_in.shape[1])
    rows = jnp.roll(rows, shift=(-my_z, -my_x), axis=(0, 1))
    partial_value = jnp.dot(
        rows.reshape(-1, attn_in.shape[1]), wo_int, preferred_element_type=jnp.float32
    ).reshape(nz, X_RING, own_rows, width)
    by_z = ring_reduce_scatter(partial_value, groups, "x", 1)
    owned_rows = ring_reduce_scatter(by_z, groups, "z", 0)

    col_total = jnp.sum(owned_rows, axis=0, keepdims=True)
    checksum = col_total * col_scale[None, :] / own_rows
    attn_out = owned_rows * token_scale[:, None] * col_scale[None, :]
    stream = (residual.astype(jnp.float32) + attn_out).astype(jnp.bfloat16)
    normed_low = normalize(stream, norm_gain)
    levels, xscale = quantize(normed_low)
    payload = jnp.concatenate(
        [levels, jnp.broadcast_to(xscale, (own_rows, SCALE_COLS))], axis=1
    )
    split = width // 2
    over_z = ring_all_gather(payload, groups, "z", split)
    gathered = ring_all_gather(over_z, groups, "x", split)
    gathered = gathered.reshape(-1, width + SCALE_COLS)
    all_levels = gathered[:, :width]
    row_scale = gathered[:, width : width + 1].astype(jnp.float32)
    gate_sum = (
        jnp.dot(all_levels, gate_int, preferred_element_type=jnp.float32) * row_scale * gate_scale
    )
    up_sum = jnp.dot(all_levels, up_int, preferred_element_type=jnp.float32) * row_scale * up_scale
    hidden = (jax.nn.silu(gate_sum) * up_sum).astype(jnp.bfloat16)
    hidden = hidden.reshape(X_RING, nz, own_rows, -1).transpose(1, 0, 2, 3)
    hidden = jnp.roll(hidden, shift=(my_z, my_x), axis=(0, 1))
    return (hidden.reshape(-1, hidden.shape[-1]), checksum)


def solution(mesh):
    placed = (
        P("dp", "tensor"),
        P("tensor", None),
        P(),
        P(("dp", "tensor")),
        P(("dp", "tensor"), None),
        P(),
        P(None, "tensor"),
        P(None, "tensor"),
        P("tensor"),
        P("tensor"),
    )
    return jax.shard_map(
        local,
        mesh=mesh,
        in_specs=placed,
        out_specs=(P("dp", "tensor"), P(("dp", "tensor"), None)),
        check_vma=False,
    )
```

```python
import jax
import jax.numpy as jnp
from jax import lax
from jax.sharding import PartitionSpec as P

X_RING = 4
SCALE_COLS = 128


def ring_perm(groups, axis, shift):
    pairs = []
    for t in range(groups):
        z, x = divmod(t, X_RING)
        if axis == "x":
            dst = z * X_RING + (x + shift) % X_RING
        else:
            dst = ((z + shift) % (groups // X_RING)) * X_RING + x
        pairs.append((t, dst))
    return pairs


def ring_reduce_scatter(parts, groups, axis, chunk_axis):
    n = parts.shape[chunk_axis]
    half = parts.shape[-1] // 2
    left = parts[..., :half]
    right = parts[..., half:]
    take = lambda arr, j: lax.index_in_dim(arr, j % n, axis=chunk_axis, keepdims=False)
    fwd = ring_perm(groups, axis, 1)
    bwd = ring_perm(groups, axis, -1)
    acc_f = take(left, n - 1)
    acc_b = take(right, 1)
    for s in range(n - 1):
        got_f = lax.ppermute(acc_f, "tensor", fwd)
        got_b = lax.ppermute(acc_b, "tensor", bwd)
        got_f, got_b = lax.optimization_barrier((got_f, got_b))
        acc_f = got_f + take(left, n - 2 - s)
        acc_b = got_b + take(right, s + 2)
    return jnp.concatenate([acc_f, acc_b], axis=-1)


def ring_all_gather(block, groups, axis, split):
    n = X_RING if axis == "x" else groups // X_RING
    fwd = ring_perm(groups, axis, 1)
    bwd = ring_perm(groups, axis, -1)
    left = [None] * n
    right = [None] * n
    left[0] = block[..., :split]
    right[0] = block[..., split:]
    cur_f = left[0]
    cur_b = right[0]
    for s in range(n - 1):
        cur_f = lax.ppermute(cur_f, "tensor", fwd)
        cur_b = lax.ppermute(cur_b, "tensor", bwd)
        cur_f, cur_b = lax.optimization_barrier((cur_f, cur_b))
        left[n - 1 - s] = cur_f
        right[s + 1] = cur_b
    return jnp.stack([jnp.concatenate([a, b], axis=-1) for a, b in zip(left, right)])


def normalize(stream, norm_gain):
    widened = stream.astype(jnp.float32)
    inverse = lax.rsqrt(jnp.mean(widened * widened, axis=1, keepdims=True) + 1e-05)
    return (widened * inverse * norm_gain[None, :]).astype(jnp.bfloat16)


def quantize(normed_low):
    widened = lax.optimization_barrier(normed_low).astype(jnp.float32)
    largest = jnp.max(jnp.abs(widened), axis=1, keepdims=True)
    xscale = ((largest + 1e-06) / 127.0).astype(jnp.bfloat16)
    levels = jnp.floor(widened / xscale.astype(jnp.float32) + 0.5).astype(jnp.bfloat16)
    return (levels, xscale)


def local(
    attn_in,
    wo_int,
    wo_exponent,
    token_scale,
    residual,
    norm_gain,
    gate_int,
    up_int,
    gate_exponent,
    up_exponent,
):
    groups = lax.axis_size("tensor")
    nz = groups // X_RING
    own_rows = residual.shape[0]
    width = wo_int.shape[1]
    me = lax.axis_index("tensor")
    my_z = me // X_RING
    my_x = me % X_RING
    col_scale = jnp.exp2(wo_exponent.astype(jnp.float32))
    gate_scale = jnp.exp2(gate_exponent.astype(jnp.float32))[None, :]
    up_scale = jnp.exp2(up_exponent.astype(jnp.float32))[None, :]

    rows = attn_in.reshape(nz, X_RING, own_rows, attn_in.shape[1])
    rows = jnp.roll(rows, shift=(-my_z, -my_x), axis=(0, 1))
    partial_value = jnp.dot(
        rows.reshape(-1, attn_in.shape[1]), wo_int, preferred_element_type=jnp.float32
    ).reshape(nz, X_RING, own_rows, width)
    by_z = ring_reduce_scatter(partial_value, groups, "x", 1)
    owned_rows = ring_reduce_scatter(by_z, groups, "z", 0)

    col_total = jnp.sum(owned_rows, axis=0, keepdims=True)
    checksum = col_total * col_scale[None, :] / own_rows
    attn_out = owned_rows * token_scale[:, None] * col_scale[None, :]
    stream = (residual.astype(jnp.float32) + attn_out).astype(jnp.bfloat16)
    normed_low = normalize(stream, norm_gain)
    levels, xscale = quantize(normed_low)
    payload = jnp.concatenate(
        [levels, jnp.broadcast_to(xscale, (own_rows, SCALE_COLS))], axis=1
    )
    split = width // 2
    over_z = ring_all_gather(payload, groups, "z", split)
    gathered = ring_all_gather(over_z, groups, "x", split)
    gathered = gathered.reshape(-1, width + SCALE_COLS)
    all_levels = gathered[:, :width]
    row_scale = gathered[:, width : width + 1].astype(jnp.float32)
    gate_sum = (
        jnp.dot(all_levels, gate_int, preferred_element_type=jnp.float32) * row_scale * gate_scale
    )
    up_sum = jnp.dot(all_levels, up_int, preferred_element_type=jnp.float32) * row_scale * up_scale
    hidden = (jax.nn.silu(gate_sum) * up_sum).astype(jnp.bfloat16)
    hidden = hidden.reshape(X_RING, nz, own_rows, -1).transpose(1, 0, 2, 3)
    hidden = jnp.roll(hidden, shift=(my_z, my_x), axis=(0, 1))
    return (hidden.reshape(-1, hidden.shape[-1]), checksum)


def solution(mesh):
    placed = (
        P("dp", "tensor"),
        P("tensor", None),
        P(),
        P(("dp", "tensor")),
        P(("dp", "tensor"), None),
        P(),
        P(None, "tensor"),
        P(None, "tensor"),
        P("tensor"),
        P("tensor"),
    )
    return jax.shard_map(
        local,
        mesh=mesh,
        in_specs=placed,
        out_specs=(P("dp", "tensor"), P(("dp", "tensor"), None)),
        check_vma=False,
    )
```

```python
import jax
import jax.numpy as jnp
from jax import lax
from jax.sharding import PartitionSpec as P

X_RING = 4
SCALE_COLS = 128
COL_GROUPS = 2


def ring_perm(groups, axis, shift):
    pairs = []
    for t in range(groups):
        z, x = divmod(t, X_RING)
        if axis == "x":
            dst = z * X_RING + (x + shift) % X_RING
        else:
            dst = ((z + shift) % (groups // X_RING)) * X_RING + x
        pairs.append((t, dst))
    return pairs


def rs_steps(parts, axis, chunk_axis, split):
    n = parts.shape[chunk_axis]
    left = parts[..., :split]
    right = parts[..., split:]
    take = lambda arr, j: lax.index_in_dim(arr, j % n, axis=chunk_axis, keepdims=False)
    acc_f = take(left, n - 1)
    acc_b = take(right, 1)
    for s in range(n - 1):
        got_f, got_b = yield ((acc_f, axis, 1), (acc_b, axis, -1))
        acc_f = got_f + take(left, n - 2 - s)
        acc_b = got_b + take(right, s + 2)
    return jnp.concatenate([acc_f, acc_b], axis=-1)


def ag_steps(block, axis, n, split):
    left = [None] * n
    right = [None] * n
    left[0] = block[..., :split]
    right[0] = block[..., split:]
    cur_f = left[0]
    cur_b = right[0]
    for s in range(n - 1):
        cur_f, cur_b = yield ((cur_f, axis, 1), (cur_b, axis, -1))
        left[n - 1 - s] = cur_f
        right[s + 1] = cur_b
    return jnp.stack([jnp.concatenate([a, b], axis=-1) for a, b in zip(left, right)])


def rs_group(parts):
    split = parts.shape[-1] // 2
    by_z = yield from rs_steps(parts, "x", 1, split)
    return (yield from rs_steps(by_z, "z", 0, split))


def ag_group(block, nz, split):
    over_z = yield from ag_steps(block, "z", nz, split)
    return (yield from ag_steps(over_z, "x", X_RING, split))


def lockstep(gens, offsets, groups):
    reqs = [None] * len(gens)
    out = [None] * len(gens)
    done = [False] * len(gens)
    tick = 0
    while not all(done):
        active = [i for i in range(len(gens)) if not done[i] and tick >= offsets[i]]
        for i in active:
            if reqs[i] is None:
                reqs[i] = next(gens[i])
        sent = [r for i in active for r in reqs[i]]
        got = [lax.ppermute(a, "tensor", ring_perm(groups, ax, sh)) for a, ax, sh in sent]
        got = lax.optimization_barrier(tuple(got)) if got else ()
        k = 0
        for i in active:
            m = len(reqs[i])
            try:
                reqs[i] = gens[i].send(tuple(got[k : k + m]))
            except StopIteration as fin:
                out[i] = fin.value
                done[i] = True
            k += m
        tick += 1
    return out


def normalize(stream, norm_gain):
    widened = stream.astype(jnp.float32)
    inverse = lax.rsqrt(jnp.mean(widened * widened, axis=1, keepdims=True) + 1e-05)
    return (widened * inverse * norm_gain[None, :]).astype(jnp.bfloat16)


def quantize(normed_low):
    widened = lax.optimization_barrier(normed_low).astype(jnp.float32)
    largest = jnp.max(jnp.abs(widened), axis=1, keepdims=True)
    xscale = ((largest + 1e-06) / 127.0).astype(jnp.bfloat16)
    levels = jnp.floor(widened / xscale.astype(jnp.float32) + 0.5).astype(jnp.bfloat16)
    return (levels, xscale)


def local(
    attn_in,
    wo_int,
    wo_exponent,
    token_scale,
    residual,
    norm_gain,
    gate_int,
    up_int,
    gate_exponent,
    up_exponent,
):
    groups = lax.axis_size("tensor")
    nz = groups // X_RING
    own_rows = residual.shape[0]
    width = wo_int.shape[1]
    me = lax.axis_index("tensor")
    my_z = me // X_RING
    my_x = me % X_RING
    col_scale = jnp.exp2(wo_exponent.astype(jnp.float32))
    gate_scale = jnp.exp2(gate_exponent.astype(jnp.float32))[None, :]
    up_scale = jnp.exp2(up_exponent.astype(jnp.float32))[None, :]

    rows = attn_in.reshape(nz, X_RING, own_rows, attn_in.shape[1])
    rows = jnp.roll(rows, shift=(-my_z, -my_x), axis=(0, 1)).reshape(-1, attn_in.shape[1])
    step = width // COL_GROUPS
    pieces = []
    for g in range(COL_GROUPS):
        part = jnp.dot(
            rows, wo_int[:, g * step : (g + 1) * step], preferred_element_type=jnp.float32
        )
        pieces.append(rs_group(part.reshape(nz, X_RING, own_rows, step)))
    owned = lockstep(pieces, [g * (X_RING - 1) for g in range(COL_GROUPS)], groups)
    owned_rows = jnp.concatenate(owned, axis=-1)

    col_total = jnp.sum(owned_rows, axis=0, keepdims=True)
    checksum = col_total * col_scale[None, :] / own_rows
    attn_out = owned_rows * token_scale[:, None] * col_scale[None, :]
    stream = (residual.astype(jnp.float32) + attn_out).astype(jnp.bfloat16)
    normed_low = normalize(stream, norm_gain)
    levels, xscale = quantize(normed_low)
    payload = jnp.concatenate(
        [levels, jnp.broadcast_to(xscale, (own_rows, SCALE_COLS))], axis=1
    )
    streams = []
    for g in range(COL_GROUPS):
        end = (g + 1) * step if g + 1 < COL_GROUPS else width + SCALE_COLS
        streams.append(ag_group(payload[:, g * step : end], nz, step // 2))
    gathered = lockstep(streams, [g * (nz - 1) for g in range(COL_GROUPS)], groups)
    gathered = [piece.reshape(-1, piece.shape[-1]) for piece in gathered]
    row_scale = gathered[-1][:, -SCALE_COLS:][:, :1].astype(jnp.float32)
    gate_acc = 0.0
    up_acc = 0.0
    for g, piece in enumerate(gathered):
        lv = piece[:, :step]
        gate_acc = gate_acc + jnp.dot(
            lv, gate_int[g * step : (g + 1) * step], preferred_element_type=jnp.float32
        )
        up_acc = up_acc + jnp.dot(
            lv, up_int[g * step : (g + 1) * step], preferred_element_type=jnp.float32
        )
    gate_sum = gate_acc * row_scale * gate_scale
    up_sum = up_acc * row_scale * up_scale
    hidden = (jax.nn.silu(gate_sum) * up_sum).astype(jnp.bfloat16)
    hidden = hidden.reshape(X_RING, nz, own_rows, -1).transpose(1, 0, 2, 3)
    hidden = jnp.roll(hidden, shift=(my_z, my_x), axis=(0, 1))
    return (hidden.reshape(-1, hidden.shape[-1]), checksum)


def solution(mesh):
    placed = (
        P("dp", "tensor"),
        P("tensor", None),
        P(),
        P(("dp", "tensor")),
        P(("dp", "tensor"), None),
        P(),
        P(None, "tensor"),
        P(None, "tensor"),
        P("tensor"),
        P("tensor"),
    )
    return jax.shard_map(
        local,
        mesh=mesh,
        in_specs=placed,
        out_specs=(P("dp", "tensor"), P(("dp", "tensor"), None)),
        check_vma=False,
    )
```

```python
import jax
import jax.numpy as jnp
from jax import lax
from jax.sharding import PartitionSpec as P

X_RING = 4
SCALE_COLS = 128


def ring_perm(groups, axis, shift):
    pairs = []
    for t in range(groups):
        z, x = divmod(t, X_RING)
        if axis == "x":
            dst = z * X_RING + (x + shift) % X_RING
        else:
            dst = ((z + shift) % (groups // X_RING)) * X_RING + x
        pairs.append((t, dst))
    return pairs


def ring_reduce_scatter(parts, groups, axis, chunk_axis):
    n = parts.shape[chunk_axis]
    half = parts.shape[-1] // 2
    left = parts[..., :half]
    right = parts[..., half:]
    take = lambda arr, j: lax.index_in_dim(arr, j % n, axis=chunk_axis, keepdims=False)
    fwd = ring_perm(groups, axis, 1)
    bwd = ring_perm(groups, axis, -1)
    acc_f = take(left, n - 1)
    acc_b = take(right, 1)
    for s in range(n - 1):
        got_f = lax.ppermute(acc_f, "tensor", fwd)
        got_b = lax.ppermute(acc_b, "tensor", bwd)
        got_f, got_b = lax.optimization_barrier((got_f, got_b))
        acc_f = got_f + take(left, n - 2 - s)
        acc_b = got_b + take(right, s + 2)
    return jnp.concatenate([acc_f, acc_b], axis=-1)


def ring_all_gather(block, groups, axis, split):
    n = X_RING if axis == "x" else groups // X_RING
    fwd = ring_perm(groups, axis, 1)
    bwd = ring_perm(groups, axis, -1)
    left = [None] * n
    right = [None] * n
    left[0] = block[..., :split]
    right[0] = block[..., split:]
    cur_f = left[0]
    cur_b = right[0]
    for s in range(n - 1):
        cur_f = lax.ppermute(cur_f, "tensor", fwd)
        cur_b = lax.ppermute(cur_b, "tensor", bwd)
        cur_f, cur_b = lax.optimization_barrier((cur_f, cur_b))
        left[n - 1 - s] = cur_f
        right[s + 1] = cur_b
    return jnp.stack([jnp.concatenate([a, b], axis=-1) for a, b in zip(left, right)])


def normalize(stream, norm_gain):
    widened = stream.astype(jnp.float32)
    inverse = lax.rsqrt(jnp.mean(widened * widened, axis=1, keepdims=True) + 1e-05)
    return (widened * inverse * norm_gain[None, :]).astype(jnp.bfloat16)


def quantize(normed_low):
    widened = lax.optimization_barrier(normed_low).astype(jnp.float32)
    largest = jnp.max(jnp.abs(widened), axis=1, keepdims=True)
    xscale = ((largest + 1e-06) / 127.0).astype(jnp.bfloat16)
    levels = jnp.floor(widened / xscale.astype(jnp.float32) + 0.5).astype(jnp.bfloat16)
    return (levels, xscale)


def local(
    attn_in,
    wo_int,
    wo_exponent,
    token_scale,
    residual,
    norm_gain,
    gate_int,
    up_int,
    gate_exponent,
    up_exponent,
):
    groups = lax.axis_size("tensor")
    nz = groups // X_RING
    own_rows = residual.shape[0]
    width = wo_int.shape[1]
    me = lax.axis_index("tensor")
    my_z = me // X_RING
    my_x = me % X_RING
    col_scale = jnp.exp2(wo_exponent.astype(jnp.float32))
    gate_scale = jnp.exp2(gate_exponent.astype(jnp.float32))[None, :]
    up_scale = jnp.exp2(up_exponent.astype(jnp.float32))[None, :]

    sc_cols = width // 2
    sc_part = jnp.dot(attn_in, wo_int[:, :sc_cols], preferred_element_type=jnp.float32)
    sc_rows = lax.psum_scatter(sc_part, "tensor", scatter_dimension=0, tiled=True)
    rows = attn_in.reshape(nz, X_RING, own_rows, attn_in.shape[1])
    rows = jnp.roll(rows, shift=(-my_z, -my_x), axis=(0, 1))
    partial_value = jnp.dot(
        rows.reshape(-1, attn_in.shape[1]), wo_int[:, sc_cols:], preferred_element_type=jnp.float32
    ).reshape(nz, X_RING, own_rows, width - sc_cols)
    by_z = ring_reduce_scatter(partial_value, groups, "x", 1)
    ring_rows = ring_reduce_scatter(by_z, groups, "z", 0)
    owned_rows = jnp.concatenate([sc_rows, ring_rows], axis=1)

    col_total = jnp.sum(owned_rows, axis=0, keepdims=True)
    checksum = col_total * col_scale[None, :] / own_rows
    attn_out = owned_rows * token_scale[:, None] * col_scale[None, :]
    stream = (residual.astype(jnp.float32) + attn_out).astype(jnp.bfloat16)
    normed_low = normalize(stream, norm_gain)
    levels, xscale = quantize(normed_low)
    sc_levels = lax.all_gather(levels[:, :sc_cols], "tensor", axis=0, tiled=True)
    payload = jnp.concatenate(
        [levels[:, sc_cols:], jnp.broadcast_to(xscale, (own_rows, SCALE_COLS))], axis=1
    )
    split = (width - sc_cols) // 2
    over_z = ring_all_gather(payload, groups, "z", split)
    gathered = ring_all_gather(over_z, groups, "x", split)
    gathered = gathered.reshape(-1, width - sc_cols + SCALE_COLS)
    ring_levels = gathered[:, : width - sc_cols]

    def to_absolute(rel):
        rel = rel.reshape(X_RING, nz, own_rows, -1).transpose(1, 0, 2, 3)
        return jnp.roll(rel, shift=(my_z, my_x), axis=(0, 1)).reshape(-1, rel.shape[-1])

    row_scale = to_absolute(gathered[:, width - sc_cols :][:, :1]).astype(jnp.float32)
    gate_acc = jnp.dot(sc_levels, gate_int[:sc_cols], preferred_element_type=jnp.float32) + to_absolute(
        jnp.dot(ring_levels, gate_int[sc_cols:], preferred_element_type=jnp.float32)
    )
    up_acc = jnp.dot(sc_levels, up_int[:sc_cols], preferred_element_type=jnp.float32) + to_absolute(
        jnp.dot(ring_levels, up_int[sc_cols:], preferred_element_type=jnp.float32)
    )
    gate_sum = gate_acc * row_scale * gate_scale
    up_sum = up_acc * row_scale * up_scale
    hidden = (jax.nn.silu(gate_sum) * up_sum).astype(jnp.bfloat16)
    return (hidden, checksum)


def solution(mesh):
    placed = (
        P("dp", "tensor"),
        P("tensor", None),
        P(),
        P(("dp", "tensor")),
        P(("dp", "tensor"), None),
        P(),
        P(None, "tensor"),
        P(None, "tensor"),
        P("tensor"),
        P("tensor"),
    )
    return jax.shard_map(
        local,
        mesh=mesh,
        in_specs=placed,
        out_specs=(P("dp", "tensor"), P(("dp", "tensor"), None)),
        check_vma=False,
    )
```

```python
import jax
import jax.numpy as jnp
from jax import lax
from jax.sharding import PartitionSpec as P

X_RING = 4
SCALE_COLS = 128
RING_DIR = 1


def ring_perm(groups, axis, shift):
    pairs = []
    for t in range(groups):
        z, x = divmod(t, X_RING)
        if axis == "x":
            dst = z * X_RING + (x + shift) % X_RING
        else:
            dst = ((z + shift) % (groups // X_RING)) * X_RING + x
        pairs.append((t, dst))
    return pairs


def ring_reduce_scatter(parts, groups, axis, chunk_axis):
    n = parts.shape[chunk_axis]
    take = lambda arr, j: lax.index_in_dim(arr, j % n, axis=chunk_axis, keepdims=False)
    perm = ring_perm(groups, axis, RING_DIR)
    acc = take(parts, -RING_DIR)
    for s in range(n - 1):
        got = lax.ppermute(acc, "tensor", perm)
        acc = got + take(parts, -RING_DIR * (s + 2))
    return acc


def ring_all_gather(block, groups, axis, split):
    n = X_RING if axis == "x" else groups // X_RING
    perm = ring_perm(groups, axis, RING_DIR)
    out = [None] * n
    out[0] = block
    cur = block
    for s in range(n - 1):
        cur = lax.ppermute(cur, "tensor", perm)
        out[(-RING_DIR * (s + 1)) % n] = cur
    return jnp.stack(out)


def normalize(stream, norm_gain):
    widened = stream.astype(jnp.float32)
    inverse = lax.rsqrt(jnp.mean(widened * widened, axis=1, keepdims=True) + 1e-05)
    return (widened * inverse * norm_gain[None, :]).astype(jnp.bfloat16)


def quantize(normed_low):
    widened = lax.optimization_barrier(normed_low).astype(jnp.float32)
    largest = jnp.max(jnp.abs(widened), axis=1, keepdims=True)
    xscale = ((largest + 1e-06) / 127.0).astype(jnp.bfloat16)
    levels = jnp.floor(widened / xscale.astype(jnp.float32) + 0.5).astype(jnp.bfloat16)
    return (levels, xscale)


def local(
    attn_in,
    wo_int,
    wo_exponent,
    token_scale,
    residual,
    norm_gain,
    gate_int,
    up_int,
    gate_exponent,
    up_exponent,
):
    groups = lax.axis_size("tensor")
    nz = groups // X_RING
    own_rows = residual.shape[0]
    width = wo_int.shape[1]
    me = lax.axis_index("tensor")
    my_z = me // X_RING
    my_x = me % X_RING
    col_scale = jnp.exp2(wo_exponent.astype(jnp.float32))
    gate_scale = jnp.exp2(gate_exponent.astype(jnp.float32))[None, :]
    up_scale = jnp.exp2(up_exponent.astype(jnp.float32))[None, :]

    sc_cols = width // 2
    sc_part = jnp.dot(attn_in, wo_int[:, :sc_cols], preferred_element_type=jnp.float32)
    sc_rows = lax.psum_scatter(sc_part, "tensor", scatter_dimension=0, tiled=True)
    rows = attn_in.reshape(nz, X_RING, own_rows, attn_in.shape[1])
    rows = jnp.roll(rows, shift=(-my_z, -my_x), axis=(0, 1))
    partial_value = jnp.dot(
        rows.reshape(-1, attn_in.shape[1]), wo_int[:, sc_cols:], preferred_element_type=jnp.float32
    ).reshape(nz, X_RING, own_rows, width - sc_cols)
    by_z = ring_reduce_scatter(partial_value, groups, "x", 1)
    ring_rows = ring_reduce_scatter(by_z, groups, "z", 0)
    owned_rows = jnp.concatenate([sc_rows, ring_rows], axis=1)

    col_total = jnp.sum(owned_rows, axis=0, keepdims=True)
    checksum = col_total * col_scale[None, :] / own_rows
    attn_out = owned_rows * token_scale[:, None] * col_scale[None, :]
    stream = (residual.astype(jnp.float32) + attn_out).astype(jnp.bfloat16)
    normed_low = normalize(stream, norm_gain)
    levels, xscale = quantize(normed_low)
    sc_levels = lax.all_gather(levels[:, :sc_cols], "tensor", axis=0, tiled=True)
    payload = jnp.concatenate(
        [levels[:, sc_cols:], jnp.broadcast_to(xscale, (own_rows, SCALE_COLS))], axis=1
    )
    split = (width - sc_cols) // 2
    over_z = ring_all_gather(payload, groups, "z", split)
    gathered = ring_all_gather(over_z, groups, "x", split)
    gathered = gathered.reshape(-1, width - sc_cols + SCALE_COLS)
    ring_levels = gathered[:, : width - sc_cols]

    def to_absolute(rel):
        rel = rel.reshape(X_RING, nz, own_rows, -1).transpose(1, 0, 2, 3)
        return jnp.roll(rel, shift=(my_z, my_x), axis=(0, 1)).reshape(-1, rel.shape[-1])

    row_scale = to_absolute(gathered[:, width - sc_cols :][:, :1]).astype(jnp.float32)
    gate_acc = jnp.dot(sc_levels, gate_int[:sc_cols], preferred_element_type=jnp.float32) + to_absolute(
        jnp.dot(ring_levels, gate_int[sc_cols:], preferred_element_type=jnp.float32)
    )
    up_acc = jnp.dot(sc_levels, up_int[:sc_cols], preferred_element_type=jnp.float32) + to_absolute(
        jnp.dot(ring_levels, up_int[sc_cols:], preferred_element_type=jnp.float32)
    )
    gate_sum = gate_acc * row_scale * gate_scale
    up_sum = up_acc * row_scale * up_scale
    hidden = (jax.nn.silu(gate_sum) * up_sum).astype(jnp.bfloat16)
    return (hidden, checksum)


def solution(mesh):
    placed = (
        P("dp", "tensor"),
        P("tensor", None),
        P(),
        P(("dp", "tensor")),
        P(("dp", "tensor"), None),
        P(),
        P(None, "tensor"),
        P(None, "tensor"),
        P("tensor"),
        P("tensor"),
    )
    return jax.shard_map(
        local,
        mesh=mesh,
        in_specs=placed,
        out_specs=(P("dp", "tensor"), P(("dp", "tensor"), None)),
        check_vma=False,
    )
```

```python
import jax
import jax.numpy as jnp
from jax import lax
from jax.sharding import PartitionSpec as P

X_RING = 4
SCALE_COLS = 128
RING_DIR = -1


def ring_perm(groups, axis, shift):
    pairs = []
    for t in range(groups):
        z, x = divmod(t, X_RING)
        if axis == "x":
            dst = z * X_RING + (x + shift) % X_RING
        else:
            dst = ((z + shift) % (groups // X_RING)) * X_RING + x
        pairs.append((t, dst))
    return pairs


def ring_reduce_scatter(parts, groups, axis, chunk_axis):
    n = parts.shape[chunk_axis]
    take = lambda arr, j: lax.index_in_dim(arr, j % n, axis=chunk_axis, keepdims=False)
    perm = ring_perm(groups, axis, RING_DIR)
    acc = take(parts, -RING_DIR)
    for s in range(n - 1):
        got = lax.ppermute(acc, "tensor", perm)
        acc = got + take(parts, -RING_DIR * (s + 2))
    return acc


def ring_all_gather(block, groups, axis, split):
    n = X_RING if axis == "x" else groups // X_RING
    perm = ring_perm(groups, axis, RING_DIR)
    out = [None] * n
    out[0] = block
    cur = block
    for s in range(n - 1):
        cur = lax.ppermute(cur, "tensor", perm)
        out[(-RING_DIR * (s + 1)) % n] = cur
    return jnp.stack(out)


def normalize(stream, norm_gain):
    widened = stream.astype(jnp.float32)
    inverse = lax.rsqrt(jnp.mean(widened * widened, axis=1, keepdims=True) + 1e-05)
    return (widened * inverse * norm_gain[None, :]).astype(jnp.bfloat16)


def quantize(normed_low):
    widened = lax.optimization_barrier(normed_low).astype(jnp.float32)
    largest = jnp.max(jnp.abs(widened), axis=1, keepdims=True)
    xscale = ((largest + 1e-06) / 127.0).astype(jnp.bfloat16)
    levels = jnp.floor(widened / xscale.astype(jnp.float32) + 0.5).astype(jnp.bfloat16)
    return (levels, xscale)


def local(
    attn_in,
    wo_int,
    wo_exponent,
    token_scale,
    residual,
    norm_gain,
    gate_int,
    up_int,
    gate_exponent,
    up_exponent,
):
    groups = lax.axis_size("tensor")
    nz = groups // X_RING
    own_rows = residual.shape[0]
    width = wo_int.shape[1]
    me = lax.axis_index("tensor")
    my_z = me // X_RING
    my_x = me % X_RING
    col_scale = jnp.exp2(wo_exponent.astype(jnp.float32))
    gate_scale = jnp.exp2(gate_exponent.astype(jnp.float32))[None, :]
    up_scale = jnp.exp2(up_exponent.astype(jnp.float32))[None, :]

    sc_cols = width // 2
    sc_part = jnp.dot(attn_in, wo_int[:, :sc_cols], preferred_element_type=jnp.float32)
    sc_rows = lax.psum_scatter(sc_part, "tensor", scatter_dimension=0, tiled=True)
    rows = attn_in.reshape(nz, X_RING, own_rows, attn_in.shape[1])
    rows = jnp.roll(rows, shift=(-my_z, -my_x), axis=(0, 1))
    partial_value = jnp.dot(
        rows.reshape(-1, attn_in.shape[1]), wo_int[:, sc_cols:], preferred_element_type=jnp.float32
    ).reshape(nz, X_RING, own_rows, width - sc_cols)
    by_z = ring_reduce_scatter(partial_value, groups, "x", 1)
    ring_rows = ring_reduce_scatter(by_z, groups, "z", 0)
    owned_rows = jnp.concatenate([sc_rows, ring_rows], axis=1)

    col_total = jnp.sum(owned_rows, axis=0, keepdims=True)
    checksum = col_total * col_scale[None, :] / own_rows
    attn_out = owned_rows * token_scale[:, None] * col_scale[None, :]
    stream = (residual.astype(jnp.float32) + attn_out).astype(jnp.bfloat16)
    normed_low = normalize(stream, norm_gain)
    levels, xscale = quantize(normed_low)
    sc_levels = lax.all_gather(levels[:, :sc_cols], "tensor", axis=0, tiled=True)
    payload = jnp.concatenate(
        [levels[:, sc_cols:], jnp.broadcast_to(xscale, (own_rows, SCALE_COLS))], axis=1
    )
    split = (width - sc_cols) // 2
    over_z = ring_all_gather(payload, groups, "z", split)
    gathered = ring_all_gather(over_z, groups, "x", split)
    gathered = gathered.reshape(-1, width - sc_cols + SCALE_COLS)
    ring_levels = gathered[:, : width - sc_cols]

    def to_absolute(rel):
        rel = rel.reshape(X_RING, nz, own_rows, -1).transpose(1, 0, 2, 3)
        return jnp.roll(rel, shift=(my_z, my_x), axis=(0, 1)).reshape(-1, rel.shape[-1])

    row_scale = to_absolute(gathered[:, width - sc_cols :][:, :1]).astype(jnp.float32)
    gate_acc = jnp.dot(sc_levels, gate_int[:sc_cols], preferred_element_type=jnp.float32) + to_absolute(
        jnp.dot(ring_levels, gate_int[sc_cols:], preferred_element_type=jnp.float32)
    )
    up_acc = jnp.dot(sc_levels, up_int[:sc_cols], preferred_element_type=jnp.float32) + to_absolute(
        jnp.dot(ring_levels, up_int[sc_cols:], preferred_element_type=jnp.float32)
    )
    gate_sum = gate_acc * row_scale * gate_scale
    up_sum = up_acc * row_scale * up_scale
    hidden = (jax.nn.silu(gate_sum) * up_sum).astype(jnp.bfloat16)
    return (hidden, checksum)


def solution(mesh):
    placed = (
        P("dp", "tensor"),
        P("tensor", None),
        P(),
        P(("dp", "tensor")),
        P(("dp", "tensor"), None),
        P(),
        P(None, "tensor"),
        P(None, "tensor"),
        P("tensor"),
        P("tensor"),
    )
    return jax.shard_map(
        local,
        mesh=mesh,
        in_specs=placed,
        out_specs=(P("dp", "tensor"), P(("dp", "tensor"), None)),
        check_vma=False,
    )
```

```python
import jax
import jax.numpy as jnp
from jax import lax
from jax.sharding import PartitionSpec as P

X_RING = 4
SCALE_COLS = 128


def ring_perm(groups, axis, shift):
    pairs = []
    for t in range(groups):
        z, x = divmod(t, X_RING)
        if axis == "x":
            dst = z * X_RING + (x + shift) % X_RING
        else:
            dst = ((z + shift) % (groups // X_RING)) * X_RING + x
        pairs.append((t, dst))
    return pairs


def ring_reduce_scatter(parts, groups, axis, chunk_axis):
    n = parts.shape[chunk_axis]
    half = parts.shape[-1] // 2
    left = parts[..., :half]
    right = parts[..., half:]
    take = lambda arr, j: lax.index_in_dim(arr, j % n, axis=chunk_axis, keepdims=False)
    fwd = ring_perm(groups, axis, 1)
    bwd = ring_perm(groups, axis, -1)
    acc_f = take(left, n - 1)
    acc_b = take(right, 1)
    for s in range(n - 1):
        got_f = lax.ppermute(acc_f, "tensor", fwd)
        got_b = lax.ppermute(acc_b, "tensor", bwd)
        got_f, got_b = lax.optimization_barrier((got_f, got_b))
        acc_f = got_f + take(left, n - 2 - s)
        acc_b = got_b + take(right, s + 2)
    return jnp.concatenate([acc_f, acc_b], axis=-1)


def ring_all_gather(block, groups, axis, split):
    n = X_RING if axis == "x" else groups // X_RING
    fwd = ring_perm(groups, axis, 1)
    bwd = ring_perm(groups, axis, -1)
    left = [None] * n
    right = [None] * n
    left[0] = block[..., :split]
    right[0] = block[..., split:]
    cur_f = left[0]
    cur_b = right[0]
    for s in range(n - 1):
        cur_f = lax.ppermute(cur_f, "tensor", fwd)
        cur_b = lax.ppermute(cur_b, "tensor", bwd)
        cur_f, cur_b = lax.optimization_barrier((cur_f, cur_b))
        left[n - 1 - s] = cur_f
        right[s + 1] = cur_b
    return jnp.stack([jnp.concatenate([a, b], axis=-1) for a, b in zip(left, right)])


def normalize(stream, norm_gain):
    widened = stream.astype(jnp.float32)
    inverse = lax.rsqrt(jnp.mean(widened * widened, axis=1, keepdims=True) + 1e-05)
    return (widened * inverse * norm_gain[None, :]).astype(jnp.bfloat16)


def quantize(normed_low):
    widened = lax.optimization_barrier(normed_low).astype(jnp.float32)
    largest = jnp.max(jnp.abs(widened), axis=1, keepdims=True)
    xscale = ((largest + 1e-06) / 127.0).astype(jnp.bfloat16)
    levels = jnp.floor(widened / xscale.astype(jnp.float32) + 0.5).astype(jnp.bfloat16)
    return (levels, xscale)


def local(
    attn_in,
    wo_int,
    wo_exponent,
    token_scale,
    residual,
    norm_gain,
    gate_int,
    up_int,
    gate_exponent,
    up_exponent,
):
    groups = lax.axis_size("tensor")
    nz = groups // X_RING
    own_rows = residual.shape[0]
    width = wo_int.shape[1]
    me = lax.axis_index("tensor")
    my_z = me // X_RING
    my_x = me % X_RING
    col_scale = jnp.exp2(wo_exponent.astype(jnp.float32))
    gate_scale = jnp.exp2(gate_exponent.astype(jnp.float32))[None, :]
    up_scale = jnp.exp2(up_exponent.astype(jnp.float32))[None, :]

    sc_cols = width * 7 // 16
    sc_part = jnp.dot(attn_in, wo_int[:, :sc_cols], preferred_element_type=jnp.float32)
    sc_rows = lax.psum_scatter(sc_part, "tensor", scatter_dimension=0, tiled=True)
    rows = attn_in.reshape(nz, X_RING, own_rows, attn_in.shape[1])
    rows = jnp.roll(rows, shift=(-my_z, -my_x), axis=(0, 1))
    partial_value = jnp.dot(
        rows.reshape(-1, attn_in.shape[1]), wo_int[:, sc_cols:], preferred_element_type=jnp.float32
    ).reshape(nz, X_RING, own_rows, width - sc_cols)
    by_z = ring_reduce_scatter(partial_value, groups, "x", 1)
    ring_rows = ring_reduce_scatter(by_z, groups, "z", 0)
    owned_rows = jnp.concatenate([sc_rows, ring_rows], axis=1)

    col_total = jnp.sum(owned_rows, axis=0, keepdims=True)
    checksum = col_total * col_scale[None, :] / own_rows
    attn_out = owned_rows * token_scale[:, None] * col_scale[None, :]
    stream = (residual.astype(jnp.float32) + attn_out).astype(jnp.bfloat16)
    normed_low = normalize(stream, norm_gain)
    levels, xscale = quantize(normed_low)
    sc_cols = width // 2
    sc_levels = lax.all_gather(levels[:, :sc_cols], "tensor", axis=0, tiled=True)
    payload = jnp.concatenate(
        [levels[:, sc_cols:], jnp.broadcast_to(xscale, (own_rows, SCALE_COLS))], axis=1
    )
    split = (width - sc_cols) // 2
    over_z = ring_all_gather(payload, groups, "z", split)
    gathered = ring_all_gather(over_z, groups, "x", split)
    gathered = gathered.reshape(-1, width - sc_cols + SCALE_COLS)
    ring_levels = gathered[:, : width - sc_cols]

    def to_absolute(rel):
        rel = rel.reshape(X_RING, nz, own_rows, -1).transpose(1, 0, 2, 3)
        return jnp.roll(rel, shift=(my_z, my_x), axis=(0, 1)).reshape(-1, rel.shape[-1])

    row_scale = to_absolute(gathered[:, width - sc_cols :][:, :1]).astype(jnp.float32)
    gate_acc = jnp.dot(sc_levels, gate_int[:sc_cols], preferred_element_type=jnp.float32) + to_absolute(
        jnp.dot(ring_levels, gate_int[sc_cols:], preferred_element_type=jnp.float32)
    )
    up_acc = jnp.dot(sc_levels, up_int[:sc_cols], preferred_element_type=jnp.float32) + to_absolute(
        jnp.dot(ring_levels, up_int[sc_cols:], preferred_element_type=jnp.float32)
    )
    gate_sum = gate_acc * row_scale * gate_scale
    up_sum = up_acc * row_scale * up_scale
    hidden = (jax.nn.silu(gate_sum) * up_sum).astype(jnp.bfloat16)
    return (hidden, checksum)


def solution(mesh):
    placed = (
        P("dp", "tensor"),
        P("tensor", None),
        P(),
        P(("dp", "tensor")),
        P(("dp", "tensor"), None),
        P(),
        P(None, "tensor"),
        P(None, "tensor"),
        P("tensor"),
        P("tensor"),
    )
    return jax.shard_map(
        local,
        mesh=mesh,
        in_specs=placed,
        out_specs=(P("dp", "tensor"), P(("dp", "tensor"), None)),
        check_vma=False,
    )
```

```python
import jax
import jax.numpy as jnp
from jax import lax
from jax.sharding import PartitionSpec as P

X_RING = 4
SCALE_COLS = 128


def ring_perm(groups, axis, shift):
    pairs = []
    for t in range(groups):
        z, x = divmod(t, X_RING)
        if axis == "x":
            dst = z * X_RING + (x + shift) % X_RING
        else:
            dst = ((z + shift) % (groups // X_RING)) * X_RING + x
        pairs.append((t, dst))
    return pairs


def ring_reduce_scatter(parts, groups, axis, chunk_axis):
    n = parts.shape[chunk_axis]
    half = parts.shape[-1] // 2
    left = parts[..., :half]
    right = parts[..., half:]
    take = lambda arr, j: lax.index_in_dim(arr, j % n, axis=chunk_axis, keepdims=False)
    fwd = ring_perm(groups, axis, 1)
    bwd = ring_perm(groups, axis, -1)
    acc_f = take(left, n - 1)
    acc_b = take(right, 1)
    for s in range(n - 1):
        got_f = lax.ppermute(acc_f, "tensor", fwd)
        got_b = lax.ppermute(acc_b, "tensor", bwd)
        got_f, got_b = lax.optimization_barrier((got_f, got_b))
        acc_f = got_f + take(left, n - 2 - s)
        acc_b = got_b + take(right, s + 2)
    return jnp.concatenate([acc_f, acc_b], axis=-1)


def ring_all_gather(block, groups, axis, split):
    n = X_RING if axis == "x" else groups // X_RING
    fwd = ring_perm(groups, axis, 1)
    bwd = ring_perm(groups, axis, -1)
    left = [None] * n
    right = [None] * n
    left[0] = block[..., :split]
    right[0] = block[..., split:]
    cur_f = left[0]
    cur_b = right[0]
    for s in range(n - 1):
        cur_f = lax.ppermute(cur_f, "tensor", fwd)
        cur_b = lax.ppermute(cur_b, "tensor", bwd)
        cur_f, cur_b = lax.optimization_barrier((cur_f, cur_b))
        left[n - 1 - s] = cur_f
        right[s + 1] = cur_b
    return jnp.stack([jnp.concatenate([a, b], axis=-1) for a, b in zip(left, right)])


def normalize(stream, norm_gain):
    widened = stream.astype(jnp.float32)
    inverse = lax.rsqrt(jnp.mean(widened * widened, axis=1, keepdims=True) + 1e-05)
    return (widened * inverse * norm_gain[None, :]).astype(jnp.bfloat16)


def quantize(normed_low):
    widened = lax.optimization_barrier(normed_low).astype(jnp.float32)
    largest = jnp.max(jnp.abs(widened), axis=1, keepdims=True)
    xscale = ((largest + 1e-06) / 127.0).astype(jnp.bfloat16)
    levels = jnp.floor(widened / xscale.astype(jnp.float32) + 0.5).astype(jnp.bfloat16)
    return (levels, xscale)


def local(
    attn_in,
    wo_int,
    wo_exponent,
    token_scale,
    residual,
    norm_gain,
    gate_int,
    up_int,
    gate_exponent,
    up_exponent,
):
    groups = lax.axis_size("tensor")
    nz = groups // X_RING
    own_rows = residual.shape[0]
    width = wo_int.shape[1]
    me = lax.axis_index("tensor")
    my_z = me // X_RING
    my_x = me % X_RING
    col_scale = jnp.exp2(wo_exponent.astype(jnp.float32))
    gate_scale = jnp.exp2(gate_exponent.astype(jnp.float32))[None, :]
    up_scale = jnp.exp2(up_exponent.astype(jnp.float32))[None, :]

    sc_cols = width // 2
    sc_part = jnp.dot(attn_in, wo_int[:, :sc_cols], preferred_element_type=jnp.float32)
    sc_rows = lax.psum_scatter(sc_part, "tensor", scatter_dimension=0, tiled=True)
    rows = attn_in.reshape(nz, X_RING, own_rows, attn_in.shape[1])
    rows = jnp.roll(rows, shift=(-my_z, -my_x), axis=(0, 1))
    partial_value = jnp.dot(
        rows.reshape(-1, attn_in.shape[1]), wo_int[:, sc_cols:], preferred_element_type=jnp.float32
    ).reshape(nz, X_RING, own_rows, width - sc_cols)
    by_x = ring_reduce_scatter(partial_value, groups, "z", 0)
    ring_rows = ring_reduce_scatter(by_x, groups, "x", 0)
    owned_rows = jnp.concatenate([sc_rows, ring_rows], axis=1)

    col_total = jnp.sum(owned_rows, axis=0, keepdims=True)
    checksum = col_total * col_scale[None, :] / own_rows
    attn_out = owned_rows * token_scale[:, None] * col_scale[None, :]
    stream = (residual.astype(jnp.float32) + attn_out).astype(jnp.bfloat16)
    normed_low = normalize(stream, norm_gain)
    levels, xscale = quantize(normed_low)
    sc_cols = width // 2
    sc_levels = lax.all_gather(levels[:, :sc_cols], "tensor", axis=0, tiled=True)
    payload = jnp.concatenate(
        [levels[:, sc_cols:], jnp.broadcast_to(xscale, (own_rows, SCALE_COLS))], axis=1
    )
    split = (width - sc_cols) // 2
    over_z = ring_all_gather(payload, groups, "z", split)
    gathered = ring_all_gather(over_z, groups, "x", split)
    gathered = gathered.reshape(-1, width - sc_cols + SCALE_COLS)
    ring_levels = gathered[:, : width - sc_cols]

    def to_absolute(rel):
        rel = rel.reshape(X_RING, nz, own_rows, -1).transpose(1, 0, 2, 3)
        return jnp.roll(rel, shift=(my_z, my_x), axis=(0, 1)).reshape(-1, rel.shape[-1])

    row_scale = to_absolute(gathered[:, width - sc_cols :][:, :1]).astype(jnp.float32)
    gate_acc = jnp.dot(sc_levels, gate_int[:sc_cols], preferred_element_type=jnp.float32) + to_absolute(
        jnp.dot(ring_levels, gate_int[sc_cols:], preferred_element_type=jnp.float32)
    )
    up_acc = jnp.dot(sc_levels, up_int[:sc_cols], preferred_element_type=jnp.float32) + to_absolute(
        jnp.dot(ring_levels, up_int[sc_cols:], preferred_element_type=jnp.float32)
    )
    gate_sum = gate_acc * row_scale * gate_scale
    up_sum = up_acc * row_scale * up_scale
    hidden = (jax.nn.silu(gate_sum) * up_sum).astype(jnp.bfloat16)
    return (hidden, checksum)


def solution(mesh):
    placed = (
        P("dp", "tensor"),
        P("tensor", None),
        P(),
        P(("dp", "tensor")),
        P(("dp", "tensor"), None),
        P(),
        P(None, "tensor"),
        P(None, "tensor"),
        P("tensor"),
        P("tensor"),
    )
    return jax.shard_map(
        local,
        mesh=mesh,
        in_specs=placed,
        out_specs=(P("dp", "tensor"), P(("dp", "tensor"), None)),
        check_vma=False,
    )
```

```python
import jax
import jax.numpy as jnp
from jax import lax
from jax.sharding import PartitionSpec as P

X_RING = 4
SCALE_COLS = 128


def ring_perm(groups, axis, shift):
    pairs = []
    for t in range(groups):
        z, x = divmod(t, X_RING)
        if axis == "x":
            dst = z * X_RING + (x + shift) % X_RING
        else:
            dst = ((z + shift) % (groups // X_RING)) * X_RING + x
        pairs.append((t, dst))
    return pairs


def ring_reduce_scatter(parts, groups, axis, chunk_axis):
    n = parts.shape[chunk_axis]
    half = parts.shape[-1] // 2
    left = parts[..., :half]
    right = parts[..., half:]
    take = lambda arr, j: lax.index_in_dim(arr, j % n, axis=chunk_axis, keepdims=False)
    fwd = ring_perm(groups, axis, 1)
    bwd = ring_perm(groups, axis, -1)
    acc_f = take(left, n - 1)
    acc_b = take(right, 1)
    for s in range(n - 1):
        got_f = lax.ppermute(acc_f, "tensor", fwd)
        got_b = lax.ppermute(acc_b, "tensor", bwd)
        got_f, got_b = lax.optimization_barrier((got_f, got_b))
        acc_f = got_f + take(left, n - 2 - s)
        acc_b = got_b + take(right, s + 2)
    return jnp.concatenate([acc_f, acc_b], axis=-1)


def ring_all_gather(block, groups, axis, split):
    n = X_RING if axis == "x" else groups // X_RING
    fwd = ring_perm(groups, axis, 1)
    bwd = ring_perm(groups, axis, -1)
    left = [None] * n
    right = [None] * n
    left[0] = block[..., :split]
    right[0] = block[..., split:]
    cur_f = left[0]
    cur_b = right[0]
    for s in range(n - 1):
        cur_f = lax.ppermute(cur_f, "tensor", fwd)
        cur_b = lax.ppermute(cur_b, "tensor", bwd)
        cur_f, cur_b = lax.optimization_barrier((cur_f, cur_b))
        left[n - 1 - s] = cur_f
        right[s + 1] = cur_b
    return jnp.stack([jnp.concatenate([a, b], axis=-1) for a, b in zip(left, right)])


def normalize(stream, norm_gain):
    widened = stream.astype(jnp.float32)
    inverse = lax.rsqrt(jnp.mean(widened * widened, axis=1, keepdims=True) + 1e-05)
    return (widened * inverse * norm_gain[None, :]).astype(jnp.bfloat16)


def quantize(normed_low):
    widened = lax.optimization_barrier(normed_low).astype(jnp.float32)
    largest = jnp.max(jnp.abs(widened), axis=1, keepdims=True)
    xscale = ((largest + 1e-06) / 127.0).astype(jnp.bfloat16)
    levels = jnp.floor(widened / xscale.astype(jnp.float32) + 0.5).astype(jnp.bfloat16)
    return (levels, xscale)


def local(
    attn_in,
    wo_int,
    wo_exponent,
    token_scale,
    residual,
    norm_gain,
    gate_int,
    up_int,
    gate_exponent,
    up_exponent,
):
    groups = lax.axis_size("tensor")
    nz = groups // X_RING
    own_rows = residual.shape[0]
    width = wo_int.shape[1]
    me = lax.axis_index("tensor")
    my_z = me // X_RING
    my_x = me % X_RING
    col_scale = jnp.exp2(wo_exponent.astype(jnp.float32))
    gate_scale = jnp.exp2(gate_exponent.astype(jnp.float32))[None, :]
    up_scale = jnp.exp2(up_exponent.astype(jnp.float32))[None, :]

    sc_cols = width // 2
    sc_part = jnp.dot(attn_in, wo_int[:, :sc_cols], preferred_element_type=jnp.float32)
    sc_rows = lax.psum_scatter(sc_part, "tensor", scatter_dimension=0, tiled=True)
    rows = attn_in.reshape(nz, X_RING, own_rows, attn_in.shape[1])
    rows = jnp.roll(rows, shift=(-my_z, -my_x), axis=(0, 1))
    partial_value = jnp.dot(
        rows.reshape(-1, attn_in.shape[1]), wo_int[:, sc_cols:], preferred_element_type=jnp.float32
    ).reshape(nz, X_RING, own_rows, width - sc_cols)
    by_z = ring_reduce_scatter(partial_value, groups, "x", 1)
    ring_rows = ring_reduce_scatter(by_z, groups, "z", 0)
    owned_rows = jnp.concatenate([sc_rows, ring_rows], axis=1)

    col_total = jnp.sum(owned_rows, axis=0, keepdims=True)
    checksum = col_total * col_scale[None, :] / own_rows
    attn_out = owned_rows * token_scale[:, None] * col_scale[None, :]
    stream = (residual.astype(jnp.float32) + attn_out).astype(jnp.bfloat16)
    normed_low = normalize(stream, norm_gain)
    levels, xscale = quantize(normed_low)
    sc_cols = width * 3 // 8
    sc_levels = lax.all_gather(levels[:, :sc_cols], "tensor", axis=0, tiled=True)
    payload = jnp.concatenate(
        [levels[:, sc_cols:], jnp.broadcast_to(xscale, (own_rows, SCALE_COLS))], axis=1
    )
    split = (width - sc_cols) // 2
    over_z = ring_all_gather(payload, groups, "z", split)
    gathered = ring_all_gather(over_z, groups, "x", split)
    gathered = gathered.reshape(-1, width - sc_cols + SCALE_COLS)
    ring_levels = gathered[:, : width - sc_cols]

    def to_absolute(rel):
        rel = rel.reshape(X_RING, nz, own_rows, -1).transpose(1, 0, 2, 3)
        return jnp.roll(rel, shift=(my_z, my_x), axis=(0, 1)).reshape(-1, rel.shape[-1])

    row_scale = to_absolute(gathered[:, width - sc_cols :][:, :1]).astype(jnp.float32)
    gate_acc = jnp.dot(sc_levels, gate_int[:sc_cols], preferred_element_type=jnp.float32) + to_absolute(
        jnp.dot(ring_levels, gate_int[sc_cols:], preferred_element_type=jnp.float32)
    )
    up_acc = jnp.dot(sc_levels, up_int[:sc_cols], preferred_element_type=jnp.float32) + to_absolute(
        jnp.dot(ring_levels, up_int[sc_cols:], preferred_element_type=jnp.float32)
    )
    gate_sum = gate_acc * row_scale * gate_scale
    up_sum = up_acc * row_scale * up_scale
    hidden = (jax.nn.silu(gate_sum) * up_sum).astype(jnp.bfloat16)
    return (hidden, checksum)


def solution(mesh):
    placed = (
        P("dp", "tensor"),
        P("tensor", None),
        P(),
        P(("dp", "tensor")),
        P(("dp", "tensor"), None),
        P(),
        P(None, "tensor"),
        P(None, "tensor"),
        P("tensor"),
        P("tensor"),
    )
    return jax.shard_map(
        local,
        mesh=mesh,
        in_specs=placed,
        out_specs=(P("dp", "tensor"), P(("dp", "tensor"), None)),
        check_vma=False,
    )
```

```python
import jax
import jax.numpy as jnp
from jax import lax
from jax.sharding import PartitionSpec as P

X_RING = 4
SCALE_COLS = 128


def ring_perm(groups, axis, shift):
    pairs = []
    for t in range(groups):
        z, x = divmod(t, X_RING)
        if axis == "x":
            dst = z * X_RING + (x + shift) % X_RING
        else:
            dst = ((z + shift) % (groups // X_RING)) * X_RING + x
        pairs.append((t, dst))
    return pairs


def ring_reduce_scatter(parts, groups, axis, chunk_axis):
    n = parts.shape[chunk_axis]
    half = parts.shape[-1] // 2
    left = parts[..., :half]
    right = parts[..., half:]
    take = lambda arr, j: lax.index_in_dim(arr, j % n, axis=chunk_axis, keepdims=False)
    fwd = ring_perm(groups, axis, 1)
    bwd = ring_perm(groups, axis, -1)
    acc_f = take(left, n - 1)
    acc_b = take(right, 1)
    for s in range(n - 1):
        got_f = lax.ppermute(acc_f, "tensor", fwd)
        got_b = lax.ppermute(acc_b, "tensor", bwd)
        got_f, got_b = lax.optimization_barrier((got_f, got_b))
        acc_f = got_f + take(left, n - 2 - s)
        acc_b = got_b + take(right, s + 2)
    return jnp.concatenate([acc_f, acc_b], axis=-1)


def ring_all_gather(block, groups, axis, split):
    n = X_RING if axis == "x" else groups // X_RING
    fwd = ring_perm(groups, axis, 1)
    bwd = ring_perm(groups, axis, -1)
    left = [None] * n
    right = [None] * n
    left[0] = block[..., :split]
    right[0] = block[..., split:]
    cur_f = left[0]
    cur_b = right[0]
    for s in range(n - 1):
        cur_f = lax.ppermute(cur_f, "tensor", fwd)
        cur_b = lax.ppermute(cur_b, "tensor", bwd)
        cur_f, cur_b = lax.optimization_barrier((cur_f, cur_b))
        left[n - 1 - s] = cur_f
        right[s + 1] = cur_b
    return jnp.stack([jnp.concatenate([a, b], axis=-1) for a, b in zip(left, right)])


def normalize(stream, norm_gain):
    widened = stream.astype(jnp.float32)
    inverse = lax.rsqrt(jnp.mean(widened * widened, axis=1, keepdims=True) + 1e-05)
    return (widened * inverse * norm_gain[None, :]).astype(jnp.bfloat16)


def quantize(normed_low):
    widened = lax.optimization_barrier(normed_low).astype(jnp.float32)
    largest = jnp.max(jnp.abs(widened), axis=1, keepdims=True)
    xscale = ((largest + 1e-06) / 127.0).astype(jnp.bfloat16)
    levels = jnp.floor(widened / xscale.astype(jnp.float32) + 0.5).astype(jnp.bfloat16)
    return (levels, xscale)


def local(
    attn_in,
    wo_int,
    wo_exponent,
    token_scale,
    residual,
    norm_gain,
    gate_int,
    up_int,
    gate_exponent,
    up_exponent,
):
    groups = lax.axis_size("tensor")
    nz = groups // X_RING
    own_rows = residual.shape[0]
    width = wo_int.shape[1]
    me = lax.axis_index("tensor")
    my_z = me // X_RING
    my_x = me % X_RING
    col_scale = jnp.exp2(wo_exponent.astype(jnp.float32))
    gate_scale = jnp.exp2(gate_exponent.astype(jnp.float32))[None, :]
    up_scale = jnp.exp2(up_exponent.astype(jnp.float32))[None, :]

    sc_cols = width // 2
    sc_part = jnp.dot(attn_in, wo_int[:, :sc_cols], preferred_element_type=jnp.float32)
    sc_rows = lax.psum_scatter(sc_part, "tensor", scatter_dimension=0, tiled=True)
    rows = attn_in.reshape(nz, X_RING, own_rows, attn_in.shape[1])
    rows = jnp.roll(rows, shift=(-my_z, -my_x), axis=(0, 1))
    partial_value = jnp.dot(
        rows.reshape(-1, attn_in.shape[1]), wo_int[:, sc_cols:], preferred_element_type=jnp.float32
    ).reshape(nz, X_RING, own_rows, width - sc_cols)
    by_z = ring_reduce_scatter(partial_value, groups, "x", 1)
    ring_rows = ring_reduce_scatter(by_z, groups, "z", 0)
    owned_rows = jnp.concatenate([sc_rows, ring_rows], axis=1)

    col_total = jnp.sum(owned_rows, axis=0, keepdims=True)
    checksum = col_total * col_scale[None, :] / own_rows
    attn_out = owned_rows * token_scale[:, None] * col_scale[None, :]
    stream = (residual.astype(jnp.float32) + attn_out).astype(jnp.bfloat16)
    normed_low = normalize(stream, norm_gain)
    levels, xscale = quantize(normed_low)
    sc_cols = width * 5 // 8
    sc_levels = lax.all_gather(levels[:, :sc_cols], "tensor", axis=0, tiled=True)
    payload = jnp.concatenate(
        [levels[:, sc_cols:], jnp.broadcast_to(xscale, (own_rows, SCALE_COLS))], axis=1
    )
    split = (width - sc_cols) // 2
    over_z = ring_all_gather(payload, groups, "z", split)
    gathered = ring_all_gather(over_z, groups, "x", split)
    gathered = gathered.reshape(-1, width - sc_cols + SCALE_COLS)
    ring_levels = gathered[:, : width - sc_cols]

    def to_absolute(rel):
        rel = rel.reshape(X_RING, nz, own_rows, -1).transpose(1, 0, 2, 3)
        return jnp.roll(rel, shift=(my_z, my_x), axis=(0, 1)).reshape(-1, rel.shape[-1])

    row_scale = to_absolute(gathered[:, width - sc_cols :][:, :1]).astype(jnp.float32)
    gate_acc = jnp.dot(sc_levels, gate_int[:sc_cols], preferred_element_type=jnp.float32) + to_absolute(
        jnp.dot(ring_levels, gate_int[sc_cols:], preferred_element_type=jnp.float32)
    )
    up_acc = jnp.dot(sc_levels, up_int[:sc_cols], preferred_element_type=jnp.float32) + to_absolute(
        jnp.dot(ring_levels, up_int[sc_cols:], preferred_element_type=jnp.float32)
    )
    gate_sum = gate_acc * row_scale * gate_scale
    up_sum = up_acc * row_scale * up_scale
    hidden = (jax.nn.silu(gate_sum) * up_sum).astype(jnp.bfloat16)
    return (hidden, checksum)


def solution(mesh):
    placed = (
        P("dp", "tensor"),
        P("tensor", None),
        P(),
        P(("dp", "tensor")),
        P(("dp", "tensor"), None),
        P(),
        P(None, "tensor"),
        P(None, "tensor"),
        P("tensor"),
        P("tensor"),
    )
    return jax.shard_map(
        local,
        mesh=mesh,
        in_specs=placed,
        out_specs=(P("dp", "tensor"), P(("dp", "tensor"), None)),
        check_vma=False,
    )
```

```python
import jax
import jax.numpy as jnp
from jax import lax
from jax.sharding import PartitionSpec as P

X_RING = 4
SCALE_COLS = 128


def ring_perm(groups, axis, shift):
    pairs = []
    for t in range(groups):
        z, x = divmod(t, X_RING)
        if axis == "x":
            dst = z * X_RING + (x + shift) % X_RING
        else:
            dst = ((z + shift) % (groups // X_RING)) * X_RING + x
        pairs.append((t, dst))
    return pairs


def ring_reduce_scatter(parts, groups, axis, chunk_axis):
    n = parts.shape[chunk_axis]
    half = parts.shape[-1] // 2
    left = parts[..., :half]
    right = parts[..., half:]
    take = lambda arr, j: lax.index_in_dim(arr, j % n, axis=chunk_axis, keepdims=False)
    fwd = ring_perm(groups, axis, 1)
    bwd = ring_perm(groups, axis, -1)
    acc_f = take(left, n - 1)
    acc_b = take(right, 1)
    for s in range(n - 1):
        got_f = lax.ppermute(acc_f, "tensor", fwd)
        got_b = lax.ppermute(acc_b, "tensor", bwd)
        got_f, got_b = lax.optimization_barrier((got_f, got_b))
        acc_f = got_f + take(left, n - 2 - s)
        acc_b = got_b + take(right, s + 2)
    return jnp.concatenate([acc_f, acc_b], axis=-1)


def ring_all_gather(block, groups, axis, split):
    n = X_RING if axis == "x" else groups // X_RING
    fwd = ring_perm(groups, axis, 1)
    bwd = ring_perm(groups, axis, -1)
    left = [None] * n
    right = [None] * n
    left[0] = block[..., :split]
    right[0] = block[..., split:]
    cur_f = left[0]
    cur_b = right[0]
    for s in range(n - 1):
        cur_f = lax.ppermute(cur_f, "tensor", fwd)
        cur_b = lax.ppermute(cur_b, "tensor", bwd)
        cur_f, cur_b = lax.optimization_barrier((cur_f, cur_b))
        left[n - 1 - s] = cur_f
        right[s + 1] = cur_b
    return jnp.stack([jnp.concatenate([a, b], axis=-1) for a, b in zip(left, right)])


def normalize(stream, norm_gain):
    widened = stream.astype(jnp.float32)
    inverse = lax.rsqrt(jnp.mean(widened * widened, axis=1, keepdims=True) + 1e-05)
    return (widened * inverse * norm_gain[None, :]).astype(jnp.bfloat16)


def quantize(normed_low):
    widened = lax.optimization_barrier(normed_low).astype(jnp.float32)
    largest = jnp.max(jnp.abs(widened), axis=1, keepdims=True)
    xscale = ((largest + 1e-06) / 127.0).astype(jnp.bfloat16)
    levels = jnp.floor(widened / xscale.astype(jnp.float32) + 0.5).astype(jnp.bfloat16)
    return (levels, xscale)


def local(
    attn_in,
    wo_int,
    wo_exponent,
    token_scale,
    residual,
    norm_gain,
    gate_int,
    up_int,
    gate_exponent,
    up_exponent,
):
    groups = lax.axis_size("tensor")
    nz = groups // X_RING
    own_rows = residual.shape[0]
    width = wo_int.shape[1]
    me = lax.axis_index("tensor")
    my_z = me // X_RING
    my_x = me % X_RING
    col_scale = jnp.exp2(wo_exponent.astype(jnp.float32))
    gate_scale = jnp.exp2(gate_exponent.astype(jnp.float32))[None, :]
    up_scale = jnp.exp2(up_exponent.astype(jnp.float32))[None, :]

    sc_cols = width // 2
    sc_part = jnp.dot(attn_in, wo_int[:, :sc_cols], preferred_element_type=jnp.float32)
    sc_rows = lax.psum_scatter(sc_part, "tensor", scatter_dimension=0, tiled=True)
    rows = attn_in.reshape(nz, X_RING, own_rows, attn_in.shape[1])
    rows = jnp.roll(rows, shift=(-my_z, -my_x), axis=(0, 1))
    partial_value = jnp.dot(
        rows.reshape(-1, attn_in.shape[1]), wo_int[:, sc_cols:], preferred_element_type=jnp.float32
    ).reshape(nz, X_RING, own_rows, width - sc_cols)
    by_z = ring_reduce_scatter(partial_value, groups, "x", 1)
    ring_rows = ring_reduce_scatter(by_z, groups, "z", 0)
    owned_rows = jnp.concatenate([sc_rows, ring_rows], axis=1)

    col_total = jnp.sum(owned_rows, axis=0, keepdims=True)
    checksum = col_total * col_scale[None, :] / own_rows
    attn_out = owned_rows * token_scale[:, None] * col_scale[None, :]
    stream = (residual.astype(jnp.float32) + attn_out).astype(jnp.bfloat16)
    normed_low = normalize(stream, norm_gain)
    levels, xscale = quantize(normed_low)
    sc_cols = width * 9 // 16
    sc_levels = lax.all_gather(levels[:, :sc_cols], "tensor", axis=0, tiled=True)
    payload = jnp.concatenate(
        [levels[:, sc_cols:], jnp.broadcast_to(xscale, (own_rows, SCALE_COLS))], axis=1
    )
    split = (width - sc_cols) // 2
    over_z = ring_all_gather(payload, groups, "z", split)
    gathered = ring_all_gather(over_z, groups, "x", split)
    gathered = gathered.reshape(-1, width - sc_cols + SCALE_COLS)
    ring_levels = gathered[:, : width - sc_cols]

    def to_absolute(rel):
        rel = rel.reshape(X_RING, nz, own_rows, -1).transpose(1, 0, 2, 3)
        return jnp.roll(rel, shift=(my_z, my_x), axis=(0, 1)).reshape(-1, rel.shape[-1])

    row_scale = to_absolute(gathered[:, width - sc_cols :][:, :1]).astype(jnp.float32)
    gate_acc = jnp.dot(sc_levels, gate_int[:sc_cols], preferred_element_type=jnp.float32) + to_absolute(
        jnp.dot(ring_levels, gate_int[sc_cols:], preferred_element_type=jnp.float32)
    )
    up_acc = jnp.dot(sc_levels, up_int[:sc_cols], preferred_element_type=jnp.float32) + to_absolute(
        jnp.dot(ring_levels, up_int[sc_cols:], preferred_element_type=jnp.float32)
    )
    gate_sum = gate_acc * row_scale * gate_scale
    up_sum = up_acc * row_scale * up_scale
    hidden = (jax.nn.silu(gate_sum) * up_sum).astype(jnp.bfloat16)
    return (hidden, checksum)


def solution(mesh):
    placed = (
        P("dp", "tensor"),
        P("tensor", None),
        P(),
        P(("dp", "tensor")),
        P(("dp", "tensor"), None),
        P(),
        P(None, "tensor"),
        P(None, "tensor"),
        P("tensor"),
        P("tensor"),
    )
    return jax.shard_map(
        local,
        mesh=mesh,
        in_specs=placed,
        out_specs=(P("dp", "tensor"), P(("dp", "tensor"), None)),
        check_vma=False,
    )
```

```python
import jax
import jax.numpy as jnp
from jax import lax
from jax.sharding import PartitionSpec as P

X_RING = 4
SCALE_COLS = 128


def ring_perm(groups, axis, shift):
    pairs = []
    for t in range(groups):
        z, x = divmod(t, X_RING)
        if axis == "x":
            dst = z * X_RING + (x + shift) % X_RING
        else:
            dst = ((z + shift) % (groups // X_RING)) * X_RING + x
        pairs.append((t, dst))
    return pairs


def ring_reduce_scatter(parts, groups, axis, chunk_axis):
    n = parts.shape[chunk_axis]
    half = parts.shape[-1] // 2
    left = parts[..., :half]
    right = parts[..., half:]
    take = lambda arr, j: lax.index_in_dim(arr, j % n, axis=chunk_axis, keepdims=False)
    fwd = ring_perm(groups, axis, 1)
    bwd = ring_perm(groups, axis, -1)
    acc_f = take(left, n - 1)
    acc_b = take(right, 1)
    for s in range(n - 1):
        got_f = lax.ppermute(acc_f, "tensor", fwd)
        got_b = lax.ppermute(acc_b, "tensor", bwd)
        got_f, got_b = lax.optimization_barrier((got_f, got_b))
        acc_f = got_f + take(left, n - 2 - s)
        acc_b = got_b + take(right, s + 2)
    return jnp.concatenate([acc_f, acc_b], axis=-1)


def ring_all_gather(block, groups, axis, split):
    n = X_RING if axis == "x" else groups // X_RING
    fwd = ring_perm(groups, axis, 1)
    bwd = ring_perm(groups, axis, -1)
    left = [None] * n
    right = [None] * n
    left[0] = block[..., :split]
    right[0] = block[..., split:]
    cur_f = left[0]
    cur_b = right[0]
    for s in range(n - 1):
        cur_f = lax.ppermute(cur_f, "tensor", fwd)
        cur_b = lax.ppermute(cur_b, "tensor", bwd)
        cur_f, cur_b = lax.optimization_barrier((cur_f, cur_b))
        left[n - 1 - s] = cur_f
        right[s + 1] = cur_b
    return jnp.stack([jnp.concatenate([a, b], axis=-1) for a, b in zip(left, right)])


def normalize(stream, norm_gain):
    widened = stream.astype(jnp.float32)
    inverse = lax.rsqrt(jnp.mean(widened * widened, axis=1, keepdims=True) + 1e-05)
    return (widened * inverse * norm_gain[None, :]).astype(jnp.bfloat16)


def quantize(normed_low):
    widened = lax.optimization_barrier(normed_low).astype(jnp.float32)
    largest = jnp.max(jnp.abs(widened), axis=1, keepdims=True)
    xscale = ((largest + 1e-06) / 127.0).astype(jnp.bfloat16)
    levels = jnp.floor(widened / xscale.astype(jnp.float32) + 0.5).astype(jnp.bfloat16)
    return (levels, xscale)


def local(
    attn_in,
    wo_int,
    wo_exponent,
    token_scale,
    residual,
    norm_gain,
    gate_int,
    up_int,
    gate_exponent,
    up_exponent,
):
    groups = lax.axis_size("tensor")
    nz = groups // X_RING
    own_rows = residual.shape[0]
    width = wo_int.shape[1]
    me = lax.axis_index("tensor")
    my_z = me // X_RING
    my_x = me % X_RING
    col_scale = jnp.exp2(wo_exponent.astype(jnp.float32))
    gate_scale = jnp.exp2(gate_exponent.astype(jnp.float32))[None, :]
    up_scale = jnp.exp2(up_exponent.astype(jnp.float32))[None, :]

    sc_cols = width // 2
    sc_part = jnp.dot(attn_in, wo_int[:, :sc_cols], preferred_element_type=jnp.float32)
    sc_rows = lax.psum_scatter(sc_part, "tensor", scatter_dimension=0, tiled=True)
    rows = attn_in.reshape(nz, X_RING, own_rows, attn_in.shape[1])
    rows = jnp.roll(rows, shift=(-my_z, -my_x), axis=(0, 1))
    partial_value = jnp.dot(
        rows.reshape(-1, attn_in.shape[1]), wo_int[:, sc_cols:], preferred_element_type=jnp.float32
    ).reshape(nz, X_RING, own_rows, width - sc_cols)
    by_z = ring_reduce_scatter(partial_value, groups, "x", 1)
    ring_rows = ring_reduce_scatter(by_z, groups, "z", 0)
    owned_rows = jnp.concatenate([sc_rows, ring_rows], axis=1)

    col_total = jnp.sum(owned_rows, axis=0, keepdims=True)
    checksum = col_total * col_scale[None, :] / own_rows
    attn_out = owned_rows * token_scale[:, None] * col_scale[None, :]
    stream = (residual.astype(jnp.float32) + attn_out).astype(jnp.bfloat16)
    normed_low = normalize(stream, norm_gain)
    levels, xscale = quantize(normed_low)
    sc_cols = width * 5 // 8
    sc_levels = lax.all_gather(levels[:, :sc_cols], "tensor", axis=0, tiled=True)
    payload = jnp.concatenate(
        [levels[:, sc_cols:], jnp.broadcast_to(xscale, (own_rows, SCALE_COLS))], axis=1
    )
    split = (width - sc_cols) // 2
    over_z = ring_all_gather(payload, groups, "z", split)
    gathered = ring_all_gather(over_z, groups, "x", split)
    gathered = gathered.reshape(-1, width - sc_cols + SCALE_COLS)
    ring_levels = gathered[:, : width - sc_cols]

    def to_absolute(rel):
        rel = rel.reshape(X_RING, nz, own_rows, -1).transpose(1, 0, 2, 3)
        return jnp.roll(rel, shift=(my_z, my_x), axis=(0, 1)).reshape(-1, rel.shape[-1])

    row_scale = to_absolute(gathered[:, width - sc_cols :][:, :1]).astype(jnp.float32)
    ff = gate_int.shape[1]
    sc_weights = jnp.concatenate([gate_int[:sc_cols], up_int[:sc_cols]], axis=1)
    ring_weights = jnp.concatenate([gate_int[sc_cols:], up_int[sc_cols:]], axis=1)
    both = jnp.dot(sc_levels, sc_weights, preferred_element_type=jnp.float32) + to_absolute(
        jnp.dot(ring_levels, ring_weights, preferred_element_type=jnp.float32)
    )
    gate_acc = both[:, :ff]
    up_acc = both[:, ff:]
    gate_sum = gate_acc * row_scale * gate_scale
    up_sum = up_acc * row_scale * up_scale
    hidden = (jax.nn.silu(gate_sum) * up_sum).astype(jnp.bfloat16)
    return (hidden, checksum)


def solution(mesh):
    placed = (
        P("dp", "tensor"),
        P("tensor", None),
        P(),
        P(("dp", "tensor")),
        P(("dp", "tensor"), None),
        P(),
        P(None, "tensor"),
        P(None, "tensor"),
        P("tensor"),
        P("tensor"),
    )
    return jax.shard_map(
        local,
        mesh=mesh,
        in_specs=placed,
        out_specs=(P("dp", "tensor"), P(("dp", "tensor"), None)),
        check_vma=False,
    )
```
